256 devices in a mesh: tm: 16 (over z, core), tile: 16 (over x, y).
Axes of the slice: x: 4, y: 4, z: 8, core: 2. Of those that a mesh axis runs over, the one named last changes fastest.
Arguments:
- obs_values: bfloat16 [16, 32768, 128], P('tm', 'tile'), may hold values from -6 to 6
- obs_weight: bfloat16 [16, 32768, 128], P('tm', 'tile'), may hold values from 0.19921875 to 2
- obs_count: int32 [16, 32768], P('tm', 'tile'), may hold values from 32 to 128
- dest_tile: int32 [16, 32768, 1], P('tm', 'tile'), may hold values from 0 to 15; in each aligned block of 2048 rows (0 to 2047, 2048 to 4095, ..., all dimensions but the last counted through in order) at most 256 rows name the same one
- jac_index: int32 [16, 32768], P('tm', 'tile'), may hold values from 0 to 255
- jacobian: bfloat16 [16, 4096, 128, 128], P('tm', 'tile'), may hold values from -0.5 to 0.5
- jac_state: int32 [16, 4096], P('tm', 'tile'), may hold values from 0 to 63
- corr_blocks: bfloat16 [16, 768, 128, 128], P('tm', 'tile'), may hold values from -0.625 to 0.625
- corr_row: int32 [16, 768], P('tm', 'tile'), may hold values from 0 to 63
- corr_col: int32 [16, 768], P('tm', 'tile'), may hold values from 0 to 63
- time_coupling: bfloat16 [16, 1024, 128], P('tm', 'tile'), may hold values from 0.19921875 to 0.59765625
Outputs:
- product: bfloat16 [16, 32768, 128], P('tm', 'tile')
The draws below stay inside these ranges and needn't reach their ends.
Inputs may be any that keep to these rules, and one draw needn't show every extreme that they name: `dest_tile`: in the rows of one device, no tile is named by more than 256 observation blocks, a bound that some block reaches.
All inputs are finite; a program needn't handle non-finite values.
Results may differ from the reference program's by a relative error of at most 0.0075.
Values may be sent and summed in bfloat16 or wider, within the bound.
No kernel may reach another device: no remote copies, remote signals or barrier semaphores. Data moves between devices by JAX's collectives and lax.ppermute only.
A program may use at most 64 MiB of HBM per device.

```python
import math
import jax
import jax.numpy as jnp
import numpy as np
from jax import lax

BLOCK = 128
OBS_DEV = 2048
JAC_DEV = 256
STATE_DEV = 64
CORR_DEV = 48
TILES = 16
WINDOWS = 16
CAP = 256
OBS_ROW = 32768
JAC_ROW = 4096
STATE_ROW = 1024
CORR_ROW = 768


def touch_ends(values, own_key, smallest, top_value):
    longest = values.shape.index(max(values.shape))
    spots = []
    for shift in (0, 1):
        where = [jax.random.randint(jax.random.fold_in(own_key, axis), (), 0, length) for axis, length in enumerate(values.shape)]
        where[longest] = (where[longest] + shift) % values.shape[longest]
        spots.append(tuple(where))
    return values.at[spots[0]].set(smallest).at[spots[1]].set(top_value)


def steps_of(stream_key, shape, pieces, least, high):
    def one(position, blocks):
        draws = jax.random.uniform(jax.random.fold_in(jax.random.fold_in(stream_key, 6), position), (blocks,), jnp.float32, least / len(pieces), high / len(pieces))
        return jnp.repeat(jnp.exp(draws), shape[position] // blocks).reshape((-1,) + (1,) * (len(shape) - position - 1))

    loudness = one(*pieces[0])
    for cut in pieces[1:]:
        loudness = loudness * one(*cut)
    return loudness


def shared_out(key, own, number, rows, amount, top, reach, skew):
    order = jax.random.permutation(key, amount)
    packed, common = shares(amount, rows * top, reach, skew, True), shares(amount, rows * top, reach, skew, False)
    places = jnp.arange(amount)

    def named(sizes, rotation):
        used = int((sizes > 0).sum())
        fixed = max(1, used // 4)
        moved = fixed + (places - fixed + rotation * (used - fixed)) % max(1, amount - fixed)
        return jnp.zeros((amount,), jnp.int32).at[order[jnp.where(places < fixed, places, moved)]].set(jnp.asarray(sizes, jnp.int32))

    sizes = jnp.where(number % 4 == 0, named(packed, number // 4), named(common, number - number // 4 - 1))
    mixed = jax.random.permutation(jax.random.fold_in(own, 3), amount)
    donor, taker = mixed[0:amount // 2 * 2:2], mixed[1:amount // 2 * 2:2]
    margin = jnp.minimum(sizes[donor] - 1, reach - sizes[taker]) // 2
    margin = jnp.where((donor == order[0]) | (taker == order[0]) | (sizes[taker] == 0), 0, jnp.maximum(margin, 0))
    moved = jax.random.randint(jax.random.fold_in(own, 4), (amount // 2,), 0, 1 << 20) % (margin + 1)
    sizes = sizes.at[donor].add(-moved).at[taker].add(moved)
    members = jnp.searchsorted(jnp.cumsum(sizes), jnp.arange(rows * top), side="right").astype(jnp.int32)
    table = members.reshape(top, rows).T
    table = table[jax.random.permutation(jax.random.fold_in(own, 1), rows)]
    rotation = jax.random.randint(jax.random.fold_in(own, 2), (rows, 1), 0, top)
    return jnp.take_along_axis(table, (jnp.arange(top)[None, :] + rotation) % top, axis=1)


def shares(count, total, limit, lean, full):
    loads = [(1 << 20) // math.isqrt(grade ** lean) + 1 for grade in range(1, count + 1)]
    largest = limit if full else min(limit, max(-(-total // count), total * loads[0] // sum(loads)))
    least = 1 if total - largest >= count - 1 else 0
    counts, spare = [largest] + [least] * (count - 1), total - largest - least * (count - 1)
    while spare > 0:
        movable = [i for i in range(1, count) if counts[i] < largest] or [i for i in range(1, count) if counts[i] < limit]
        pool, budget = sum([loads[i] for i in movable]), spare
        for i in movable:
            addition = min(limit - counts[i], max(1, budget * loads[i] // pool), spare)
            counts[i] = counts[i] + addition
            spare = spare - addition
    return np.array(counts)


def bell_draw(rng, shape, deviation, most, pieces=(), kind=jnp.bfloat16):
    entries = deviation * jax.random.normal(rng, shape, jnp.float32)
    if pieces:
        entries = entries * steps_of(rng, shape, pieces, -0.22, 0.18)
    return jnp.clip(entries, -most, most).astype(kind)


def setup_inputs(seed: int = 0) -> dict:
    splits = jax.random.split(jax.random.key(seed), 12)
    obs_values = bell_draw(splits[0], (WINDOWS, OBS_ROW, BLOCK), 1.0, 6.0, ((0, 16), (1, 16)))
    obs_weight = jnp.clip(jnp.exp(math.log(2.0) - 2.306499 * jax.random.uniform(splits[1], (WINDOWS, OBS_ROW, BLOCK), jnp.float32) ** steps_of(splits[1], (WINDOWS, OBS_ROW, BLOCK), ((0, 16), (1, 16)), -0.2, 0.2)), 0.19921875, 2.0).astype(jnp.bfloat16)
    obs_count = touch_ends(jax.random.randint(splits[2], (WINDOWS, OBS_ROW), BLOCK // 4, BLOCK + 1), jax.random.fold_in(splits[2], 1), BLOCK // 4, BLOCK).astype(jnp.int32)
    dest_tile_keys = jax.random.split(jax.random.fold_in(splits[3], 1), WINDOWS * OBS_ROW // OBS_DEV)
    dest_tile_turns = jax.random.permutation(jax.random.fold_in(splits[3], 3), WINDOWS * OBS_ROW // OBS_DEV)
    dest_tile = jax.vmap(lambda own, number: shared_out(jax.random.fold_in(splits[3], 2), own, number, OBS_DEV, TILES, 1, CAP, 2))(dest_tile_keys, dest_tile_turns).reshape((WINDOWS, OBS_ROW, 1))
    jac_index = touch_ends(jax.random.randint(splits[4], (WINDOWS, OBS_ROW), 0, JAC_DEV), jax.random.fold_in(splits[4], 1), 0, JAC_DEV - 1).astype(jnp.int32)
    jacobian = bell_draw(splits[5], (WINDOWS, JAC_ROW, BLOCK, BLOCK), BLOCK ** -0.5, 0.5, ((0, 16), (1, 16)))
    jac_state = touch_ends(jax.random.randint(splits[6], (WINDOWS, JAC_ROW), 0, STATE_DEV), jax.random.fold_in(splits[6], 1), 0, STATE_DEV - 1).astype(jnp.int32)
    corr_blocks = bell_draw(splits[7], (WINDOWS, CORR_ROW, BLOCK, BLOCK), (BLOCK * CORR_DEV // STATE_DEV) ** -0.5, 0.625, ((0, 16), (1, 16)))
    corr_row = touch_ends(jax.random.randint(splits[8], (WINDOWS, CORR_ROW), 0, STATE_DEV), jax.random.fold_in(splits[8], 1), 0, STATE_DEV - 1).astype(jnp.int32)
    corr_col = touch_ends(jax.random.randint(splits[9], (WINDOWS, CORR_ROW), 0, STATE_DEV), jax.random.fold_in(splits[9], 1), 0, STATE_DEV - 1).astype(jnp.int32)
    time_coupling = jnp.clip(0.19921875 + 0.3984375 * jax.random.uniform(splits[10], (WINDOWS, STATE_ROW, BLOCK), jnp.float32) ** steps_of(splits[10], (WINDOWS, STATE_ROW, BLOCK), ((0, 16), (1, 16)), -0.2, 0.2), 0.19921875, 0.59765625).astype(jnp.bfloat16)
    return {"obs_values": obs_values, "obs_weight": obs_weight, "obs_count": obs_count, "dest_tile": dest_tile, "jac_index": jac_index, "jacobian": jacobian, "jac_state": jac_state, "corr_blocks": corr_blocks, "corr_row": corr_row, "corr_col": corr_col, "time_coupling": time_coupling}


def reference(obs_values, obs_weight, obs_count, dest_tile, jac_index, jacobian, jac_state, corr_blocks, corr_row, corr_col, time_coupling):
    lane_index = jnp.arange(BLOCK, dtype=jnp.int32)
    keeping = (lane_index[None, None, :] < obs_count[:, :, None]).astype(jnp.float32)
    weighted = (obs_values.astype(jnp.float32) * obs_weight.astype(jnp.float32) * keeping).astype(jnp.bfloat16)
    bin_index = (dest_tile[:, :, 0] * JAC_DEV + jac_index).astype(jnp.int32)
    jac_tiles = jnp.arange(JAC_ROW, dtype=jnp.int32) // JAC_DEV
    state_index = (jac_tiles[None, :] * STATE_DEV + jac_state).astype(jnp.int32)
    corr_tiles = jnp.arange(CORR_ROW, dtype=jnp.int32) // CORR_DEV
    write_index = (corr_tiles[None, :] * STATE_DEV + corr_row).astype(jnp.int32)
    read_index = (corr_tiles[None, :] * STATE_DEV + corr_col).astype(jnp.int32)

    def spatial_part(inputs):
        weighted_t, bins_t, jac_t, state_t, corr_t, writes_t, reads_t = inputs
        summed = jax.ops.segment_sum(weighted_t.astype(jnp.float32), bins_t, num_segments=JAC_ROW)
        merged = summed.astype(jnp.bfloat16)
        spread = jnp.einsum('kij,ki->kj', jac_t.astype(jnp.float32), merged.astype(jnp.float32))
        state = jax.ops.segment_sum(spread, state_t, num_segments=STATE_ROW).astype(jnp.bfloat16)
        source = state[reads_t]
        mixing = jnp.einsum('cij,cj->ci', corr_t.astype(jnp.float32), source.astype(jnp.float32))
        return jax.ops.segment_sum(mixing, writes_t, num_segments=STATE_ROW).astype(jnp.bfloat16)

    spatial = lax.map(spatial_part, (weighted, bin_index, jacobian, state_index, corr_blocks, write_index, read_index))
    blank_state = jnp.zeros_like(spatial[:1])
    earlier = jnp.concatenate([blank_state, spatial[:-1]], axis=0)
    later_state = jnp.concatenate([spatial[1:], blank_state], axis=0)
    later_coupling = jnp.concatenate([time_coupling[1:], jnp.zeros_like(time_coupling[:1])], axis=0)
    coupled = (spatial.astype(jnp.float32) + time_coupling.astype(jnp.float32) * earlier.astype(jnp.float32)
               + later_coupling.astype(jnp.float32) * later_state.astype(jnp.float32)).astype(jnp.bfloat16)

    def forward_part(inputs):
        coupled_t, jac_t, state_t, bins_t = inputs
        local_state = coupled_t[state_t]
        model_obs = jnp.einsum('kij,kj->ki', jac_t.astype(jnp.float32), local_state.astype(jnp.float32)).astype(jnp.bfloat16)
        return model_obs[bins_t]

    picked = lax.map(forward_part, (coupled, jacobian, state_index, bin_index))
    return (picked.astype(jnp.float32) * keeping).astype(jnp.bfloat16)
```

```python
import jax
import jax.numpy as jnp
from jax import lax
from jax.sharding import PartitionSpec as P

CAP = 256


def from_behind(x, axis, by):
    length = lax.axis_size(axis)
    pairs = [(i, i + by) for i in range(length) if 0 <= i + by < length]
    return lax.ppermute(x, axis, pairs)


def shards(
    obs_values,
    obs_weight,
    obs_count,
    dest_tile,
    jac_index,
    jacobian,
    jac_state,
    corr_blocks,
    corr_row,
    corr_col,
    time_coupling,
):
    obs_total = obs_values.shape[1]
    block_width = obs_values.shape[2]
    jac_total = jacobian.shape[1]
    state_total = time_coupling.shape[1]
    tiles = lax.axis_size("tile")
    slots = tiles * CAP
    lane_index = lax.broadcasted_iota(jnp.int32, (obs_total, block_width), 1)
    keeping = (lane_index < obs_count[0][:, None]).astype(jnp.float32)
    weighted = (
        obs_values[0].astype(jnp.float32) * obs_weight[0].astype(jnp.float32) * keeping
    ).astype(jnp.bfloat16)
    target = dest_tile[0, :, 0]
    column = jac_index[0]

    tile_ids = lax.broadcasted_iota(jnp.int32, (obs_total, tiles), 1)
    names = (tile_ids == target[:, None]).astype(jnp.bfloat16)
    rows = lax.broadcasted_iota(jnp.int32, (obs_total, obs_total), 0)
    cols = lax.broadcasted_iota(jnp.int32, (obs_total, obs_total), 1)
    lower = (cols <= rows).astype(jnp.bfloat16)
    counts = jnp.dot(lower, names, preferred_element_type=jnp.float32)
    rank = jnp.sum(counts * names.astype(jnp.float32), axis=1).astype(jnp.int32) - 1
    slot = target * CAP + rank

    slot_ids = lax.broadcasted_iota(jnp.int32, (slots, obs_total), 0)
    placer = (slot_ids == slot[None, :]).astype(jnp.bfloat16)
    packed = jnp.dot(placer, weighted, preferred_element_type=jnp.float32).astype(jnp.bfloat16)
    packed_col = jnp.dot(
        placer, column.astype(jnp.bfloat16)[:, None], preferred_element_type=jnp.float32
    ).astype(jnp.bfloat16)
    send = jnp.concatenate(
        [
            packed.reshape(tiles, CAP, block_width),
            packed_col.reshape(tiles, CAP // block_width, block_width),
            jnp.zeros((tiles, 16 - CAP // block_width, block_width), jnp.bfloat16),
        ],
        axis=1,
    )
    recv = lax.all_to_all(send, "tile", 0, 0, tiled=True)
    recv_rows = recv[:, :CAP].reshape(slots, block_width)
    recv_col = recv[:, CAP:CAP + CAP // block_width].reshape(1, slots).astype(jnp.int32)
    jac_ids = lax.broadcasted_iota(jnp.int32, (jac_total, slots), 0)
    binner = (jac_ids == recv_col).astype(jnp.bfloat16)
    summed = jnp.dot(binner, recv_rows, preferred_element_type=jnp.float32)

    merged = summed.astype(jnp.bfloat16)
    spread = jnp.einsum("kij,ki->kj", jacobian[0], merged, preferred_element_type=jnp.float32)
    state_ids = lax.broadcasted_iota(jnp.int32, (state_total, jac_total), 0)
    owners = state_ids == jac_state[0][None, :]
    state = jnp.dot(owners.astype(jnp.float32), spread, precision=lax.Precision.HIGHEST).astype(
        jnp.bfloat16
    )
    corr_total = corr_blocks.shape[1]
    read_ids = lax.broadcasted_iota(jnp.int32, (corr_total, state_total), 1)
    reader = (read_ids == corr_col[0][:, None]).astype(jnp.bfloat16)
    source = jnp.dot(reader, state, preferred_element_type=jnp.float32).astype(jnp.bfloat16)
    mixing = jnp.einsum("cij,cj->ci", corr_blocks[0], source, preferred_element_type=jnp.float32)
    write_ids = lax.broadcasted_iota(jnp.int32, (state_total, corr_total), 0)
    writer = (write_ids == corr_row[0][None, :]).astype(jnp.float32)
    spatial = jnp.dot(writer, mixing, precision=lax.Precision.HIGHEST).astype(jnp.bfloat16)
    coupling = time_coupling[0]
    earlier = from_behind(spatial, "tm", 1)
    later_state, later_coupling = from_behind((spatial, coupling), "tm", -1)
    coupled = (
        spatial.astype(jnp.float32)
        + coupling.astype(jnp.float32) * earlier.astype(jnp.float32)
        + later_coupling.astype(jnp.float32) * later_state.astype(jnp.float32)
    ).astype(jnp.bfloat16)
    local_state = jnp.dot(
        owners.T.astype(jnp.bfloat16), coupled, preferred_element_type=jnp.float32
    ).astype(jnp.bfloat16)
    model_obs = jnp.einsum(
        "kij,kj->ki", jacobian[0], local_state, preferred_element_type=jnp.float32
    ).astype(jnp.bfloat16)

    answer = jnp.dot(binner.T, model_obs, preferred_element_type=jnp.float32).astype(jnp.bfloat16)
    back = lax.all_to_all(answer.reshape(tiles, CAP, block_width), "tile", 0, 0, tiled=True)
    gathered = jnp.dot(
        placer.T, back.reshape(slots, block_width), preferred_element_type=jnp.float32
    )
    return (gathered * keeping).astype(jnp.bfloat16)[None]


def solution(mesh):
    in_specs = (
        P("tm", "tile", None),
        P("tm", "tile", None),
        P("tm", "tile"),
        P("tm", "tile", None),
        P("tm", "tile"),
        P("tm", "tile", None, None),
        P("tm", "tile"),
        P("tm", "tile", None, None),
        P("tm", "tile"),
        P("tm", "tile"),
        P("tm", "tile", None),
    )
    out_specs = P("tm", "tile", None)
    return jax.shard_map(shards, mesh=mesh, in_specs=in_specs, out_specs=out_specs, check_vma=False)
```

```python
import jax
import jax.numpy as jnp
from jax import lax
from jax.sharding import PartitionSpec as P

CAP = 256


def from_behind(x, axis, by):
    length = lax.axis_size(axis)
    pairs = [(i, i + by) for i in range(length) if 0 <= i + by < length]
    return lax.ppermute(x, axis, pairs)


def shards(
    obs_values,
    obs_weight,
    obs_count,
    dest_tile,
    jac_index,
    jacobian,
    jac_state,
    corr_blocks,
    corr_row,
    corr_col,
    time_coupling,
):
    obs_total = obs_values.shape[1]
    block_width = obs_values.shape[2]
    jac_total = jacobian.shape[1]
    state_total = time_coupling.shape[1]
    tiles = lax.axis_size("tile")
    slots = tiles * CAP
    lane_index = lax.broadcasted_iota(jnp.int32, (obs_total, block_width), 1)
    keeping = (lane_index < obs_count[0][:, None]).astype(jnp.float32)
    weighted = (
        obs_values[0].astype(jnp.float32) * obs_weight[0].astype(jnp.float32) * keeping
    ).astype(jnp.bfloat16)
    target = dest_tile[0, :, 0]
    column = jac_index[0]

    tile_ids = lax.broadcasted_iota(jnp.int32, (obs_total, tiles), 1)
    names = (tile_ids == target[:, None]).astype(jnp.bfloat16)
    chunk = 128
    pieces = obs_total // chunk
    rows = lax.broadcasted_iota(jnp.int32, (chunk, chunk), 0)
    cols = lax.broadcasted_iota(jnp.int32, (chunk, chunk), 1)
    lower = (cols <= rows).astype(jnp.bfloat16)
    names_c = names.reshape(pieces, chunk, tiles)
    within = jnp.einsum("rc,pct->prt", lower, names_c, preferred_element_type=jnp.float32)
    totals = within[:, chunk - 1, :]
    before = jnp.cumsum(totals, axis=0) - totals
    counts = (within + before[:, None, :]).reshape(obs_total, tiles)
    rank = jnp.sum(counts * names.astype(jnp.float32), axis=1).astype(jnp.int32) - 1
    slot = target * CAP + rank

    slot_ids = lax.broadcasted_iota(jnp.int32, (slots, obs_total), 0)
    placer = (slot_ids == slot[None, :]).astype(jnp.bfloat16)
    packed = jnp.dot(placer, weighted, preferred_element_type=jnp.float32).astype(jnp.bfloat16)
    packed_col = jnp.dot(
        placer, column.astype(jnp.bfloat16)[:, None], preferred_element_type=jnp.float32
    ).astype(jnp.bfloat16)
    send = jnp.concatenate(
        [
            packed.reshape(tiles, CAP, block_width),
            packed_col.reshape(tiles, CAP // block_width, block_width),
            jnp.zeros((tiles, 16 - CAP // block_width, block_width), jnp.bfloat16),
        ],
        axis=1,
    )
    recv = lax.all_to_all(send, "tile", 0, 0, tiled=True)
    recv_rows = recv[:, :CAP].reshape(slots, block_width)
    recv_col = recv[:, CAP:CAP + CAP // block_width].reshape(1, slots).astype(jnp.int32)
    jac_ids = lax.broadcasted_iota(jnp.int32, (jac_total, slots), 0)
    binner = (jac_ids == recv_col).astype(jnp.bfloat16)
    summed = jnp.dot(binner, recv_rows, preferred_element_type=jnp.float32)

    merged = summed.astype(jnp.bfloat16)
    spread = jnp.einsum("kij,ki->kj", jacobian[0], merged, preferred_element_type=jnp.float32)
    state_ids = lax.broadcasted_iota(jnp.int32, (state_total, jac_total), 0)
    owners = state_ids == jac_state[0][None, :]
    state = jnp.dot(owners.astype(jnp.float32), spread, precision=lax.Precision.HIGHEST).astype(
        jnp.bfloat16
    )
    corr_total = corr_blocks.shape[1]
    read_ids = lax.broadcasted_iota(jnp.int32, (corr_total, state_total), 1)
    reader = (read_ids == corr_col[0][:, None]).astype(jnp.bfloat16)
    source = jnp.dot(reader, state, preferred_element_type=jnp.float32).astype(jnp.bfloat16)
    mixing = jnp.einsum("cij,cj->ci", corr_blocks[0], source, preferred_element_type=jnp.float32)
    write_ids = lax.broadcasted_iota(jnp.int32, (state_total, corr_total), 0)
    writer = (write_ids == corr_row[0][None, :]).astype(jnp.float32)
    spatial = jnp.dot(writer, mixing, precision=lax.Precision.HIGHEST).astype(jnp.bfloat16)
    coupling = time_coupling[0]
    earlier = from_behind(spatial, "tm", 1)
    later_state, later_coupling = from_behind((spatial, coupling), "tm", -1)
    coupled = (
        spatial.astype(jnp.float32)
        + coupling.astype(jnp.float32) * earlier.astype(jnp.float32)
        + later_coupling.astype(jnp.float32) * later_state.astype(jnp.float32)
    ).astype(jnp.bfloat16)
    local_state = jnp.dot(
        owners.T.astype(jnp.bfloat16), coupled, preferred_element_type=jnp.float32
    ).astype(jnp.bfloat16)
    model_obs = jnp.einsum(
        "kij,kj->ki", jacobian[0], local_state, preferred_element_type=jnp.float32
    ).astype(jnp.bfloat16)

    answer = jnp.dot(binner.T, model_obs, preferred_element_type=jnp.float32).astype(jnp.bfloat16)
    back = lax.all_to_all(answer.reshape(tiles, CAP, block_width), "tile", 0, 0, tiled=True)
    gathered = jnp.take(back.reshape(slots, block_width), slot, axis=0, mode="clip").astype(jnp.float32)
    return (gathered * keeping).astype(jnp.bfloat16)[None]


def solution(mesh):
    in_specs = (
        P("tm", "tile", None),
        P("tm", "tile", None),
        P("tm", "tile"),
        P("tm", "tile", None),
        P("tm", "tile"),
        P("tm", "tile", None, None),
        P("tm", "tile"),
        P("tm", "tile", None, None),
        P("tm", "tile"),
        P("tm", "tile"),
        P("tm", "tile", None),
    )
    out_specs = P("tm", "tile", None)
    return jax.shard_map(shards, mesh=mesh, in_specs=in_specs, out_specs=out_specs, check_vma=False)
```

```python
import jax
import jax.numpy as jnp
from jax import lax
from jax.sharding import PartitionSpec as P

CAP = 256


def from_behind(x, axis, by):
    length = lax.axis_size(axis)
    pairs = [(i, i + by) for i in range(length) if 0 <= i + by < length]
    return lax.ppermute(x, axis, pairs)


def shards(
    obs_values,
    obs_weight,
    obs_count,
    dest_tile,
    jac_index,
    jacobian,
    jac_state,
    corr_blocks,
    corr_row,
    corr_col,
    time_coupling,
):
    obs_total = obs_values.shape[1]
    block_width = obs_values.shape[2]
    jac_total = jacobian.shape[1]
    state_total = time_coupling.shape[1]
    tiles = lax.axis_size("tile")
    slots = tiles * CAP
    lane_index = lax.broadcasted_iota(jnp.int32, (obs_total, block_width), 1)
    keeping = (lane_index < obs_count[0][:, None]).astype(jnp.float32)
    weighted = (
        obs_values[0].astype(jnp.float32) * obs_weight[0].astype(jnp.float32) * keeping
    ).astype(jnp.bfloat16)
    target = dest_tile[0, :, 0]
    column = jac_index[0]

    tile_ids = lax.broadcasted_iota(jnp.int32, (obs_total, tiles), 1)
    names = (tile_ids == target[:, None]).astype(jnp.bfloat16)
    chunk = 128
    pieces = obs_total // chunk
    rows = lax.broadcasted_iota(jnp.int32, (chunk, chunk), 0)
    cols = lax.broadcasted_iota(jnp.int32, (chunk, chunk), 1)
    lower = (cols <= rows).astype(jnp.bfloat16)
    names_c = names.reshape(pieces, chunk, tiles)
    within = jnp.einsum("rc,pct->prt", lower, names_c, preferred_element_type=jnp.float32)
    totals = within[:, chunk - 1, :]
    before = jnp.cumsum(totals, axis=0) - totals
    counts = (within + before[:, None, :]).reshape(obs_total, tiles)
    rank = jnp.sum(counts * names.astype(jnp.float32), axis=1).astype(jnp.int32) - 1
    slot = target * CAP + rank

    slot_ids = lax.broadcasted_iota(jnp.int32, (slots, obs_total), 0)
    placer = (slot_ids == slot[None, :]).astype(jnp.bfloat16)
    packed = jnp.dot(placer, weighted, preferred_element_type=jnp.float32).astype(jnp.bfloat16)
    rank_ids = lax.broadcasted_iota(jnp.int32, (obs_total, CAP), 1)
    ranked = (rank_ids == rank[:, None]).astype(jnp.bfloat16)
    packed_col = jnp.dot(
        (names * column.astype(jnp.bfloat16)[:, None]).T, ranked, preferred_element_type=jnp.float32
    ).astype(jnp.bfloat16)
    send = jnp.concatenate(
        [
            packed.reshape(tiles, CAP, block_width),
            packed_col.reshape(tiles, CAP // block_width, block_width),
            jnp.zeros((tiles, 16 - CAP // block_width, block_width), jnp.bfloat16),
        ],
        axis=1,
    )
    recv = lax.all_to_all(send, "tile", 0, 0, tiled=True)
    recv_rows = recv[:, :CAP].reshape(slots, block_width)
    recv_col = recv[:, CAP:CAP + CAP // block_width].reshape(1, slots).astype(jnp.int32)
    jac_ids = lax.broadcasted_iota(jnp.int32, (jac_total, slots), 0)
    binner = (jac_ids == recv_col).astype(jnp.bfloat16)
    summed = jnp.dot(binner, recv_rows, preferred_element_type=jnp.float32)

    merged = summed.astype(jnp.bfloat16)
    group = 16
    groups = jac_total // group
    jac_groups = jacobian[0].reshape(groups, group * block_width, block_width)
    eye = (
        lax.broadcasted_iota(jnp.int32, (group, group), 0)
        == lax.broadcasted_iota(jnp.int32, (group, group), 1)
    ).astype(jnp.bfloat16)
    spread_left = (
        merged.reshape(groups, group, 1, block_width) * eye[None, :, :, None]
    ).reshape(groups, group, group * block_width)
    spread = jnp.einsum(
        "gkr,grj->gkj", spread_left, jac_groups, preferred_element_type=jnp.float32
    ).reshape(jac_total, block_width)
    state_ids = lax.broadcasted_iota(jnp.int32, (state_total, jac_total), 0)
    owners = state_ids == jac_state[0][None, :]
    state = jnp.dot(owners.astype(jnp.float32), spread, precision=lax.Precision.HIGHEST).astype(
        jnp.bfloat16
    )
    corr_total = corr_blocks.shape[1]
    read_ids = lax.broadcasted_iota(jnp.int32, (corr_total, state_total), 1)
    reader = (read_ids == corr_col[0][:, None]).astype(jnp.bfloat16)
    source = jnp.dot(reader, state, preferred_element_type=jnp.float32).astype(jnp.bfloat16)
    mixing = jnp.einsum("cij,cj->ci", corr_blocks[0], source, preferred_element_type=jnp.float32)
    write_ids = lax.broadcasted_iota(jnp.int32, (state_total, corr_total), 0)
    writer = (write_ids == corr_row[0][None, :]).astype(jnp.float32)
    spatial = jnp.dot(writer, mixing, precision=lax.Precision.HIGHEST).astype(jnp.bfloat16)
    coupling = time_coupling[0]
    earlier = from_behind(spatial, "tm", 1)
    later_state, later_coupling = from_behind((spatial, coupling), "tm", -1)
    coupled = (
        spatial.astype(jnp.float32)
        + coupling.astype(jnp.float32) * earlier.astype(jnp.float32)
        + later_coupling.astype(jnp.float32) * later_state.astype(jnp.float32)
    ).astype(jnp.bfloat16)
    local_state = jnp.dot(
        owners.T.astype(jnp.bfloat16), coupled, preferred_element_type=jnp.float32
    ).astype(jnp.bfloat16)
    wide = jnp.einsum(
        "gkj,grj->gkr",
        local_state.reshape(groups, group, block_width),
        jac_groups,
        preferred_element_type=jnp.float32,
    ).reshape(groups, group, group, block_width)
    model_obs = (
        jnp.sum(wide * eye.astype(jnp.float32)[None, :, :, None], axis=2)
        .reshape(jac_total, block_width)
        .astype(jnp.bfloat16)
    )

    answer = jnp.dot(binner.T, model_obs, preferred_element_type=jnp.float32).astype(jnp.bfloat16)
    back = lax.all_to_all(answer.reshape(tiles, CAP, block_width), "tile", 0, 0, tiled=True)
    gathered = jnp.take(back.reshape(slots, block_width), slot, axis=0, mode="clip").astype(jnp.float32)
    return (gathered * keeping).astype(jnp.bfloat16)[None]


def solution(mesh):
    in_specs = (
        P("tm", "tile", None),
        P("tm", "tile", None),
        P("tm", "tile"),
        P("tm", "tile", None),
        P("tm", "tile"),
        P("tm", "tile", None, None),
        P("tm", "tile"),
        P("tm", "tile", None, None),
        P("tm", "tile"),
        P("tm", "tile"),
        P("tm", "tile", None),
    )
    out_specs = P("tm", "tile", None)
    return jax.shard_map(shards, mesh=mesh, in_specs=in_specs, out_specs=out_specs, check_vma=False)
```

```python
import jax
import jax.numpy as jnp
from jax import lax
from jax.sharding import PartitionSpec as P

CAP = 256


def from_behind(x, axis, by):
    length = lax.axis_size(axis)
    pairs = [(i, i + by) for i in range(length) if 0 <= i + by < length]
    return lax.ppermute(x, axis, pairs)


def shards(
    obs_values,
    obs_weight,
    obs_count,
    dest_tile,
    jac_index,
    jacobian,
    jac_state,
    corr_blocks,
    corr_row,
    corr_col,
    time_coupling,
):
    obs_total = obs_values.shape[1]
    block_width = obs_values.shape[2]
    jac_total = jacobian.shape[1]
    state_total = time_coupling.shape[1]
    tiles = lax.axis_size("tile")
    slots = tiles * CAP
    lane_index = lax.broadcasted_iota(jnp.int32, (obs_total, block_width), 1)
    keeping = (lane_index < obs_count[0][:, None]).astype(jnp.float32)
    weighted = (
        obs_values[0].astype(jnp.float32) * obs_weight[0].astype(jnp.float32) * keeping
    ).astype(jnp.bfloat16)
    target = dest_tile[0, :, 0]
    column = jac_index[0]

    tile_ids = lax.broadcasted_iota(jnp.int32, (obs_total, tiles), 1)
    names = (tile_ids == target[:, None]).astype(jnp.bfloat16)
    chunk = 128
    pieces = obs_total // chunk
    rows = lax.broadcasted_iota(jnp.int32, (chunk, chunk), 0)
    cols = lax.broadcasted_iota(jnp.int32, (chunk, chunk), 1)
    lower = (cols <= rows).astype(jnp.bfloat16)
    names_c = names.reshape(pieces, chunk, tiles)
    within = jnp.einsum("rc,pct->prt", lower, names_c, preferred_element_type=jnp.float32)
    totals = within[:, chunk - 1, :]
    before = jnp.cumsum(totals, axis=0) - totals
    counts = (within + before[:, None, :]).reshape(obs_total, tiles)
    rank = jnp.sum(counts * names.astype(jnp.float32), axis=1).astype(jnp.int32) - 1
    slot = target * CAP + rank

    slot_ids = lax.broadcasted_iota(jnp.int32, (slots, obs_total), 0)
    placer = (slot_ids == slot[None, :]).astype(jnp.bfloat16)
    packed = jnp.dot(placer, weighted, preferred_element_type=jnp.float32).astype(jnp.bfloat16)
    rank_ids = lax.broadcasted_iota(jnp.int32, (obs_total, CAP), 1)
    ranked = (rank_ids == rank[:, None]).astype(jnp.bfloat16)
    packed_col = jnp.dot(
        (names * column.astype(jnp.bfloat16)[:, None]).T, ranked, preferred_element_type=jnp.float32
    ).astype(jnp.bfloat16)
    send = jnp.concatenate(
        [
            packed.reshape(tiles, CAP, block_width),
            packed_col.reshape(tiles, CAP // block_width, block_width),
            jnp.zeros((tiles, 16 - CAP // block_width, block_width), jnp.bfloat16),
        ],
        axis=1,
    )
    recv = lax.all_to_all(send, "tile", 0, 0, tiled=True)
    recv_rows = recv[:, :CAP].reshape(slots, block_width)
    recv_col = recv[:, CAP:CAP + CAP // block_width].reshape(1, slots).astype(jnp.int32)
    jac_ids = lax.broadcasted_iota(jnp.int32, (jac_total, slots), 0)
    binner = (jac_ids == recv_col).astype(jnp.bfloat16)
    summed = jnp.dot(binner, recv_rows, preferred_element_type=jnp.float32)

    merged = summed.astype(jnp.bfloat16)
    group = 16
    groups = jac_total // group
    jac_groups = jacobian[0].reshape(groups, group * block_width, block_width)
    eye = (
        lax.broadcasted_iota(jnp.int32, (group, group), 0)
        == lax.broadcasted_iota(jnp.int32, (group, group), 1)
    ).astype(jnp.bfloat16)
    block_of = lax.broadcasted_iota(jnp.int32, (groups, group, group * block_width), 2) // block_width
    own_block = lax.broadcasted_iota(jnp.int32, (groups, group, group * block_width), 1)
    spread_left = jnp.where(
        block_of == own_block,
        jnp.tile(merged.reshape(groups, group, block_width), (1, 1, group)),
        jnp.zeros((), jnp.bfloat16),
    )
    spread = jnp.einsum(
        "gkr,grj->gkj", spread_left, jac_groups, preferred_element_type=jnp.float32
    ).reshape(jac_total, block_width)
    state_ids = lax.broadcasted_iota(jnp.int32, (state_total, jac_total), 0)
    owners = state_ids == jac_state[0][None, :]
    state = jnp.dot(owners.astype(jnp.float32), spread, precision=lax.Precision.HIGHEST).astype(
        jnp.bfloat16
    )
    corr_total = corr_blocks.shape[1]
    read_ids = lax.broadcasted_iota(jnp.int32, (corr_total, state_total), 1)
    reader = (read_ids == corr_col[0][:, None]).astype(jnp.bfloat16)
    source = jnp.dot(reader, state, preferred_element_type=jnp.float32).astype(jnp.bfloat16)
    mixing = jnp.einsum("cij,cj->ci", corr_blocks[0], source, preferred_element_type=jnp.float32)
    write_ids = lax.broadcasted_iota(jnp.int32, (state_total, corr_total), 0)
    writer = (write_ids == corr_row[0][None, :]).astype(jnp.float32)
    spatial = jnp.dot(writer, mixing, precision=lax.Precision.HIGHEST).astype(jnp.bfloat16)
    coupling = time_coupling[0]
    earlier = from_behind(spatial, "tm", 1)
    later_state, later_coupling = from_behind((spatial, coupling), "tm", -1)
    coupled = (
        spatial.astype(jnp.float32)
        + coupling.astype(jnp.float32) * earlier.astype(jnp.float32)
        + later_coupling.astype(jnp.float32) * later_state.astype(jnp.float32)
    ).astype(jnp.bfloat16)
    local_state = jnp.dot(
        owners.T.astype(jnp.bfloat16), coupled, preferred_element_type=jnp.float32
    ).astype(jnp.bfloat16)
    wide = jnp.einsum(
        "gkj,grj->gkr",
        local_state.reshape(groups, group, block_width),
        jac_groups,
        preferred_element_type=jnp.float32,
    ).reshape(groups, group, group, block_width)
    model_obs = (
        jnp.sum(wide * eye.astype(jnp.float32)[None, :, :, None], axis=2)
        .reshape(jac_total, block_width)
        .astype(jnp.bfloat16)
    )

    answer = jnp.dot(binner.T, model_obs, preferred_element_type=jnp.float32).astype(jnp.bfloat16)
    back = lax.all_to_all(answer.reshape(tiles, CAP, block_width), "tile", 0, 0, tiled=True)
    gathered = jnp.take(back.reshape(slots, block_width), slot, axis=0, mode="clip").astype(jnp.float32)
    return (gathered * keeping).astype(jnp.bfloat16)[None]


def solution(mesh):
    in_specs = (
        P("tm", "tile", None),
        P("tm", "tile", None),
        P("tm", "tile"),
        P("tm", "tile", None),
        P("tm", "tile"),
        P("tm", "tile", None, None),
        P("tm", "tile"),
        P("tm", "tile", None, None),
        P("tm", "tile"),
        P("tm", "tile"),
        P("tm", "tile", None),
    )
    out_specs = P("tm", "tile", None)
    return jax.shard_map(shards, mesh=mesh, in_specs=in_specs, out_specs=out_specs, check_vma=False)
```

```python
import jax
import jax.numpy as jnp
from jax import lax
from jax.sharding import PartitionSpec as P

CAP = 256


def from_behind(x, axis, by):
    length = lax.axis_size(axis)
    pairs = [(i, i + by) for i in range(length) if 0 <= i + by < length]
    return lax.ppermute(x, axis, pairs)


def shards(
    obs_values,
    obs_weight,
    obs_count,
    dest_tile,
    jac_index,
    jacobian,
    jac_state,
    corr_blocks,
    corr_row,
    corr_col,
    time_coupling,
):
    obs_total = obs_values.shape[1]
    block_width = obs_values.shape[2]
    jac_total = jacobian.shape[1]
    state_total = time_coupling.shape[1]
    tiles = lax.axis_size("tile")
    slots = tiles * CAP
    lane_index = lax.broadcasted_iota(jnp.int32, (obs_total, block_width), 1)
    keeping = (lane_index < obs_count[0][:, None]).astype(jnp.float32)
    weighted = (
        obs_values[0].astype(jnp.float32) * obs_weight[0].astype(jnp.float32) * keeping
    ).astype(jnp.bfloat16)
    target = dest_tile[0, :, 0]
    column = jac_index[0]

    tile_ids = lax.broadcasted_iota(jnp.int32, (obs_total, tiles), 1)
    names = (tile_ids == target[:, None]).astype(jnp.bfloat16)
    chunk = 128
    pieces = obs_total // chunk
    rows = lax.broadcasted_iota(jnp.int32, (chunk, chunk), 0)
    cols = lax.broadcasted_iota(jnp.int32, (chunk, chunk), 1)
    lower = (cols <= rows).astype(jnp.bfloat16)
    names_c = names.reshape(pieces, chunk, tiles)
    within = jnp.einsum("rc,pct->prt", lower, names_c, preferred_element_type=jnp.float32)
    totals = within[:, chunk - 1, :]
    before = jnp.cumsum(totals, axis=0) - totals
    counts = (within + before[:, None, :]).reshape(obs_total, tiles)
    rank = jnp.sum(counts * names.astype(jnp.float32), axis=1).astype(jnp.int32) - 1
    slot = target * CAP + rank

    rank_ids = lax.broadcasted_iota(jnp.int32, (obs_total, CAP), 1)
    ranked = (rank_ids == rank[:, None]).astype(jnp.bfloat16)
    packed_col = jnp.dot(
        (names * column.astype(jnp.bfloat16)[:, None]).T, ranked, preferred_element_type=jnp.float32
    ).astype(jnp.bfloat16)
    extra = 16
    stride = CAP + extra
    frame = jnp.concatenate(
        [
            jnp.zeros((tiles, CAP, block_width), jnp.bfloat16),
            packed_col.reshape(tiles, CAP // block_width, block_width),
            jnp.zeros((tiles, extra - CAP // block_width, block_width), jnp.bfloat16),
        ],
        axis=1,
    ).reshape(tiles * stride, block_width)
    send = frame.at[target * stride + rank].set(weighted, unique_indices=True).reshape(
        tiles, stride, block_width
    )
    recv = lax.all_to_all(send, "tile", 0, 0, tiled=True)
    recv_rows = recv[:, :CAP].reshape(slots, block_width)
    recv_col = recv[:, CAP:CAP + CAP // block_width].reshape(1, slots).astype(jnp.int32)
    jac_ids = lax.broadcasted_iota(jnp.int32, (jac_total, slots), 0)
    binner = (jac_ids == recv_col).astype(jnp.bfloat16)
    summed = jnp.dot(binner, recv_rows, preferred_element_type=jnp.float32)

    merged = summed.astype(jnp.bfloat16)
    group = 16
    groups = jac_total // group
    jac_groups = jacobian[0].reshape(groups, group * block_width, block_width)
    eye = (
        lax.broadcasted_iota(jnp.int32, (group, group), 0)
        == lax.broadcasted_iota(jnp.int32, (group, group), 1)
    ).astype(jnp.bfloat16)
    spread = jnp.einsum("kij,ki->kj", jacobian[0], merged, preferred_element_type=jnp.float32)
    state_ids = lax.broadcasted_iota(jnp.int32, (state_total, jac_total), 0)
    owners = state_ids == jac_state[0][None, :]
    state = jnp.dot(owners.astype(jnp.float32), spread, precision=lax.Precision.HIGHEST).astype(
        jnp.bfloat16
    )
    corr_total = corr_blocks.shape[1]
    read_ids = lax.broadcasted_iota(jnp.int32, (corr_total, state_total), 1)
    reader = (read_ids == corr_col[0][:, None]).astype(jnp.bfloat16)
    source = jnp.dot(reader, state, preferred_element_type=jnp.float32).astype(jnp.bfloat16)
    mixing = jnp.einsum("cij,cj->ci", corr_blocks[0], source, preferred_element_type=jnp.float32)
    write_ids = lax.broadcasted_iota(jnp.int32, (state_total, corr_total), 0)
    writer = (write_ids == corr_row[0][None, :]).astype(jnp.float32)
    spatial = jnp.dot(writer, mixing, precision=lax.Precision.HIGHEST).astype(jnp.bfloat16)
    coupling = time_coupling[0]
    earlier = from_behind(spatial, "tm", 1)
    later_state, later_coupling = from_behind((spatial, coupling), "tm", -1)
    coupled = (
        spatial.astype(jnp.float32)
        + coupling.astype(jnp.float32) * earlier.astype(jnp.float32)
        + later_coupling.astype(jnp.float32) * later_state.astype(jnp.float32)
    ).astype(jnp.bfloat16)
    local_state = jnp.dot(
        owners.T.astype(jnp.bfloat16), coupled, preferred_element_type=jnp.float32
    ).astype(jnp.bfloat16)
    wide = jnp.einsum(
        "gkj,grj->gkr",
        local_state.reshape(groups, group, block_width),
        jac_groups,
        preferred_element_type=jnp.float32,
    ).reshape(groups, group, group, block_width)
    model_obs = (
        jnp.sum(wide * eye.astype(jnp.float32)[None, :, :, None], axis=2)
        .reshape(jac_total, block_width)
        .astype(jnp.bfloat16)
    )

    answer = jnp.dot(binner.T, model_obs, preferred_element_type=jnp.float32).astype(jnp.bfloat16)
    back = lax.all_to_all(answer.reshape(tiles, CAP, block_width), "tile", 0, 0, tiled=True)
    gathered = jnp.take(back.reshape(slots, block_width), slot, axis=0, mode="clip").astype(jnp.float32)
    return (gathered * keeping).astype(jnp.bfloat16)[None]


def solution(mesh):
    in_specs = (
        P("tm", "tile", None),
        P("tm", "tile", None),
        P("tm", "tile"),
        P("tm", "tile", None),
        P("tm", "tile"),
        P("tm", "tile", None, None),
        P("tm", "tile"),
        P("tm", "tile", None, None),
        P("tm", "tile"),
        P("tm", "tile"),
        P("tm", "tile", None),
    )
    out_specs = P("tm", "tile", None)
    return jax.shard_map(shards, mesh=mesh, in_specs=in_specs, out_specs=out_specs, check_vma=False)
```

```python
import jax
import jax.numpy as jnp
from jax import lax
from jax.sharding import PartitionSpec as P

CAP = 256


def from_behind(x, axis, by):
    length = lax.axis_size(axis)
    pairs = [(i, i + by) for i in range(length) if 0 <= i + by < length]
    return lax.ppermute(x, axis, pairs)


def shards(
    obs_values,
    obs_weight,
    obs_count,
    dest_tile,
    jac_index,
    jacobian,
    jac_state,
    corr_blocks,
    corr_row,
    corr_col,
    time_coupling,
):
    obs_total = obs_values.shape[1]
    block_width = obs_values.shape[2]
    jac_total = jacobian.shape[1]
    state_total = time_coupling.shape[1]
    tiles = lax.axis_size("tile")
    slots = tiles * CAP
    lane_index = lax.broadcasted_iota(jnp.int32, (obs_total, block_width), 1)
    keeping = (lane_index < obs_count[0][:, None]).astype(jnp.float32)
    weighted = (
        obs_values[0].astype(jnp.float32) * obs_weight[0].astype(jnp.float32) * keeping
    ).astype(jnp.bfloat16)
    target = dest_tile[0, :, 0]
    column = jac_index[0]

    tile_ids = lax.broadcasted_iota(jnp.int32, (obs_total, tiles), 1)
    names = (tile_ids == target[:, None]).astype(jnp.bfloat16)
    chunk = 128
    pieces = obs_total // chunk
    rows = lax.broadcasted_iota(jnp.int32, (chunk, chunk), 0)
    cols = lax.broadcasted_iota(jnp.int32, (chunk, chunk), 1)
    lower = (cols <= rows).astype(jnp.bfloat16)
    names_c = names.reshape(pieces, chunk, tiles)
    within = jnp.einsum("rc,pct->prt", lower, names_c, preferred_element_type=jnp.float32)
    totals = within[:, chunk - 1, :]
    before = jnp.cumsum(totals, axis=0) - totals
    counts = (within + before[:, None, :]).reshape(obs_total, tiles)
    rank = jnp.sum(counts * names.astype(jnp.float32), axis=1).astype(jnp.int32) - 1
    slot = target * CAP + rank

    slot_ids = lax.broadcasted_iota(jnp.int32, (slots, obs_total), 0)
    placer = (slot_ids == slot[None, :]).astype(jnp.bfloat16)
    packed = jnp.dot(placer, weighted, preferred_element_type=jnp.float32).astype(jnp.bfloat16)
    rank_ids = lax.broadcasted_iota(jnp.int32, (obs_total, CAP), 1)
    ranked = (rank_ids == rank[:, None]).astype(jnp.bfloat16)
    packed_col = jnp.dot(
        (names * column.astype(jnp.bfloat16)[:, None]).T, ranked, preferred_element_type=jnp.float32
    ).astype(jnp.bfloat16)
    send = jnp.concatenate(
        [
            packed.reshape(tiles, CAP, block_width),
            packed_col.reshape(tiles, CAP // block_width, block_width),
            jnp.zeros((tiles, 16 - CAP // block_width, block_width), jnp.bfloat16),
        ],
        axis=1,
    )
    recv = lax.all_to_all(send, "tile", 0, 0, tiled=True)
    recv_rows = recv[:, :CAP].reshape(slots, block_width)
    recv_col = recv[:, CAP:CAP + CAP // block_width].reshape(1, slots).astype(jnp.int32)
    jac_ids = lax.broadcasted_iota(jnp.int32, (jac_total, slots), 0)
    binner = (jac_ids == recv_col).astype(jnp.bfloat16)
    summed = jnp.dot(binner, recv_rows, preferred_element_type=jnp.float32)

    merged = summed.astype(jnp.bfloat16)
    group = 16
    groups = jac_total // group
    jac_groups = jacobian[0].reshape(groups, group * block_width, block_width)
    eye = (
        lax.broadcasted_iota(jnp.int32, (group, group), 0)
        == lax.broadcasted_iota(jnp.int32, (group, group), 1)
    ).astype(jnp.bfloat16)
    spread = jnp.einsum("kij,ki->kj", jacobian[0], merged, preferred_element_type=jnp.float32)
    state_ids = lax.broadcasted_iota(jnp.int32, (state_total, jac_total), 0)
    owners = state_ids == jac_state[0][None, :]
    state = jnp.dot(owners.astype(jnp.float32), spread, precision=lax.Precision.HIGHEST).astype(
        jnp.bfloat16
    )
    corr_total = corr_blocks.shape[1]
    read_ids = lax.broadcasted_iota(jnp.int32, (corr_total, state_total), 1)
    reader = (read_ids == corr_col[0][:, None]).astype(jnp.bfloat16)
    source = jnp.dot(reader, state, preferred_element_type=jnp.float32).astype(jnp.bfloat16)
    mixing = jnp.einsum("cij,cj->ci", corr_blocks[0], source, preferred_element_type=jnp.float32)
    write_ids = lax.broadcasted_iota(jnp.int32, (state_total, corr_total), 0)
    writer = (write_ids == corr_row[0][None, :]).astype(jnp.float32)
    spatial = jnp.dot(writer, mixing, precision=lax.Precision.HIGHEST).astype(jnp.bfloat16)
    coupling = time_coupling[0]
    earlier = from_behind(spatial, "tm", 1)
    later_state, later_coupling = from_behind((spatial, coupling), "tm", -1)
    coupled = (
        spatial.astype(jnp.float32)
        + coupling.astype(jnp.float32) * earlier.astype(jnp.float32)
        + later_coupling.astype(jnp.float32) * later_state.astype(jnp.float32)
    ).astype(jnp.bfloat16)
    local_state = jnp.dot(
        owners.T.astype(jnp.bfloat16), coupled, preferred_element_type=jnp.float32
    ).astype(jnp.bfloat16)
    wide = jnp.einsum(
        "gkj,grj->gkr",
        local_state.reshape(groups, group, block_width),
        jac_groups,
        preferred_element_type=jnp.float32,
    ).reshape(groups, group, group, block_width)
    model_obs = (
        jnp.sum(wide * eye.astype(jnp.float32)[None, :, :, None], axis=2)
        .reshape(jac_total, block_width)
        .astype(jnp.bfloat16)
    )

    answer = jnp.dot(binner.T, model_obs, preferred_element_type=jnp.float32).astype(jnp.bfloat16)
    back = lax.all_to_all(answer.reshape(tiles, CAP, block_width), "tile", 0, 0, tiled=True)
    gathered = jnp.take(back.reshape(slots, block_width), slot, axis=0, mode="clip").astype(jnp.float32)
    return (gathered * keeping).astype(jnp.bfloat16)[None]


def solution(mesh):
    in_specs = (
        P("tm", "tile", None),
        P("tm", "tile", None),
        P("tm", "tile"),
        P("tm", "tile", None),
        P("tm", "tile"),
        P("tm", "tile", None, None),
        P("tm", "tile"),
        P("tm", "tile", None, None),
        P("tm", "tile"),
        P("tm", "tile"),
        P("tm", "tile", None),
    )
    out_specs = P("tm", "tile", None)
    return jax.shard_map(shards, mesh=mesh, in_specs=in_specs, out_specs=out_specs, check_vma=False)
```

```python
import jax
import jax.numpy as jnp
from jax import lax
from jax.sharding import PartitionSpec as P

CAP = 256


def from_behind(x, axis, by):
    length = lax.axis_size(axis)
    pairs = [(i, i + by) for i in range(length) if 0 <= i + by < length]
    return lax.ppermute(x, axis, pairs)


def shards(
    obs_values,
    obs_weight,
    obs_count,
    dest_tile,
    jac_index,
    jacobian,
    jac_state,
    corr_blocks,
    corr_row,
    corr_col,
    time_coupling,
):
    obs_total = obs_values.shape[1]
    block_width = obs_values.shape[2]
    jac_total = jacobian.shape[1]
    state_total = time_coupling.shape[1]
    tiles = lax.axis_size("tile")
    slots = tiles * CAP
    lane_index = lax.broadcasted_iota(jnp.int32, (obs_total, block_width), 1)
    keeping = (lane_index < obs_count[0][:, None]).astype(jnp.float32)
    weighted = (
        obs_values[0].astype(jnp.float32) * obs_weight[0].astype(jnp.float32) * keeping
    ).astype(jnp.bfloat16)
    target = dest_tile[0, :, 0]
    column = jac_index[0]

    tile_ids = lax.broadcasted_iota(jnp.int32, (obs_total, tiles), 1)
    names = (tile_ids == target[:, None]).astype(jnp.bfloat16)
    chunk = 128
    pieces = obs_total // chunk
    rows = lax.broadcasted_iota(jnp.int32, (chunk, chunk), 0)
    cols = lax.broadcasted_iota(jnp.int32, (chunk, chunk), 1)
    lower = (cols <= rows).astype(jnp.bfloat16)
    names_c = names.reshape(pieces, chunk, tiles)
    within = jnp.einsum("rc,pct->prt", lower, names_c, preferred_element_type=jnp.float32)
    totals = within[:, chunk - 1, :]
    before = jnp.cumsum(totals, axis=0) - totals
    counts = (within + before[:, None, :]).reshape(obs_total, tiles)
    rank = jnp.sum(counts * names.astype(jnp.float32), axis=1).astype(jnp.int32) - 1
    slot = target * CAP + rank

    slot_ids = lax.broadcasted_iota(jnp.int32, (slots, obs_total), 0)
    placer = (slot_ids == slot[None, :]).astype(jnp.bfloat16)
    labelled = jnp.concatenate(
        [weighted, jnp.broadcast_to(column.astype(jnp.bfloat16)[:, None], (obs_total, block_width))],
        axis=1,
    )
    placed = jnp.dot(placer, labelled, preferred_element_type=jnp.float32).astype(jnp.bfloat16)
    packed = placed[:, :block_width]
    packed_col = placed[:, block_width]
    send = jnp.concatenate(
        [
            packed.reshape(tiles, CAP, block_width),
            packed_col.reshape(tiles, CAP // block_width, block_width),
            jnp.zeros((tiles, 16 - CAP // block_width, block_width), jnp.bfloat16),
        ],
        axis=1,
    )
    recv = lax.all_to_all(send, "tile", 0, 0, tiled=True)
    recv_rows = recv[:, :CAP].reshape(slots, block_width)
    recv_col = recv[:, CAP:CAP + CAP // block_width].reshape(1, slots).astype(jnp.int32)
    jac_ids = lax.broadcasted_iota(jnp.int32, (jac_total, slots), 0)
    binner = (jac_ids == recv_col).astype(jnp.bfloat16)
    summed = jnp.dot(binner, recv_rows, preferred_element_type=jnp.float32)

    merged = summed.astype(jnp.bfloat16)
    group = 16
    groups = jac_total // group
    jac_groups = jacobian[0].reshape(groups, group * block_width, block_width)
    eye = (
        lax.broadcasted_iota(jnp.int32, (group, group), 0)
        == lax.broadcasted_iota(jnp.int32, (group, group), 1)
    ).astype(jnp.bfloat16)
    spread = jnp.einsum("kij,ki->kj", jacobian[0], merged, preferred_element_type=jnp.float32)
    state_ids = lax.broadcasted_iota(jnp.int32, (state_total, jac_total), 0)
    owners = state_ids == jac_state[0][None, :]
    state = jnp.dot(owners.astype(jnp.float32), spread, precision=lax.Precision.HIGHEST).astype(
        jnp.bfloat16
    )
    corr_total = corr_blocks.shape[1]
    read_ids = lax.broadcasted_iota(jnp.int32, (corr_total, state_total), 1)
    reader = (read_ids == corr_col[0][:, None]).astype(jnp.bfloat16)
    source = jnp.dot(reader, state, preferred_element_type=jnp.float32).astype(jnp.bfloat16)
    mixing = jnp.einsum("cij,cj->ci", corr_blocks[0], source, preferred_element_type=jnp.float32)
    write_ids = lax.broadcasted_iota(jnp.int32, (state_total, corr_total), 0)
    writer = (write_ids == corr_row[0][None, :]).astype(jnp.float32)
    spatial = jnp.dot(writer, mixing, precision=lax.Precision.HIGHEST).astype(jnp.bfloat16)
    coupling = time_coupling[0]
    earlier = from_behind(spatial, "tm", 1)
    later_state, later_coupling = from_behind((spatial, coupling), "tm", -1)
    coupled = (
        spatial.astype(jnp.float32)
        + coupling.astype(jnp.float32) * earlier.astype(jnp.float32)
        + later_coupling.astype(jnp.float32) * later_state.astype(jnp.float32)
    ).astype(jnp.bfloat16)
    local_state = jnp.dot(
        owners.T.astype(jnp.bfloat16), coupled, preferred_element_type=jnp.float32
    ).astype(jnp.bfloat16)
    wide = jnp.einsum(
        "gkj,grj->gkr",
        local_state.reshape(groups, group, block_width),
        jac_groups,
        preferred_element_type=jnp.float32,
    ).reshape(groups, group, group, block_width)
    model_obs = (
        jnp.sum(wide * eye.astype(jnp.float32)[None, :, :, None], axis=2)
        .reshape(jac_total, block_width)
        .astype(jnp.bfloat16)
    )

    answer = jnp.dot(binner.T, model_obs, preferred_element_type=jnp.float32).astype(jnp.bfloat16)
    back = lax.all_to_all(answer.reshape(tiles, CAP, block_width), "tile", 0, 0, tiled=True)
    gathered = jnp.take(back.reshape(slots, block_width), slot, axis=0, mode="clip").astype(jnp.float32)
    return (gathered * keeping).astype(jnp.bfloat16)[None]


def solution(mesh):
    in_specs = (
        P("tm", "tile", None),
        P("tm", "tile", None),
        P("tm", "tile"),
        P("tm", "tile", None),
        P("tm", "tile"),
        P("tm", "tile", None, None),
        P("tm", "tile"),
        P("tm", "tile", None, None),
        P("tm", "tile"),
        P("tm", "tile"),
        P("tm", "tile", None),
    )
    out_specs = P("tm", "tile", None)
    return jax.shard_map(shards, mesh=mesh, in_specs=in_specs, out_specs=out_specs, check_vma=False)
```

```python
import jax
import jax.numpy as jnp
from jax import lax
from jax.sharding import PartitionSpec as P

CAP = 256


def from_behind(x, axis, by):
    length = lax.axis_size(axis)
    pairs = [(i, i + by) for i in range(length) if 0 <= i + by < length]
    return lax.ppermute(x, axis, pairs)


def shards(
    obs_values,
    obs_weight,
    obs_count,
    dest_tile,
    jac_index,
    jacobian,
    jac_state,
    corr_blocks,
    corr_row,
    corr_col,
    time_coupling,
):
    obs_total = obs_values.shape[1]
    block_width = obs_values.shape[2]
    jac_total = jacobian.shape[1]
    state_total = time_coupling.shape[1]
    tiles = lax.axis_size("tile")
    slots = tiles * CAP
    lane_index = lax.broadcasted_iota(jnp.int32, (obs_total, block_width), 1)
    keeping = (lane_index < obs_count[0][:, None]).astype(jnp.float32)
    weighted = (
        obs_values[0].astype(jnp.float32) * obs_weight[0].astype(jnp.float32) * keeping
    ).astype(jnp.bfloat16)
    target = dest_tile[0, :, 0]
    column = jac_index[0]

    tile_ids = lax.broadcasted_iota(jnp.int32, (obs_total, tiles), 1)
    names = (tile_ids == target[:, None]).astype(jnp.bfloat16)
    chunk = 128
    pieces = obs_total // chunk
    rows = lax.broadcasted_iota(jnp.int32, (chunk, chunk), 0)
    cols = lax.broadcasted_iota(jnp.int32, (chunk, chunk), 1)
    lower = (cols <= rows).astype(jnp.bfloat16)
    names_c = names.reshape(pieces, chunk, tiles)
    within = jnp.einsum("rc,pct->prt", lower, names_c, preferred_element_type=jnp.float32)
    totals = within[:, chunk - 1, :]
    before = jnp.cumsum(totals, axis=0) - totals
    counts = (within + before[:, None, :]).reshape(obs_total, tiles)
    rank = jnp.sum(counts * names.astype(jnp.float32), axis=1).astype(jnp.int32) - 1
    slot = target * CAP + rank

    rank_ids = lax.broadcasted_iota(jnp.int32, (obs_total, CAP), 1)
    ranked = (rank_ids == rank[:, None]).astype(jnp.bfloat16)
    packed_col = jnp.dot(
        (names * column.astype(jnp.bfloat16)[:, None]).T, ranked, preferred_element_type=jnp.float32
    ).astype(jnp.bfloat16)
    masked = jnp.where(
        (tile_ids == target[:, None]).T[:, :, None], weighted[None], jnp.zeros((), jnp.bfloat16)
    )
    packed = jnp.einsum(
        "jr,djc->drc", ranked, masked, preferred_element_type=jnp.float32
    ).astype(jnp.bfloat16)
    send = jnp.concatenate(
        [
            packed.reshape(tiles, CAP, block_width),
            packed_col.reshape(tiles, CAP // block_width, block_width),
            jnp.zeros((tiles, 16 - CAP // block_width, block_width), jnp.bfloat16),
        ],
        axis=1,
    )
    recv = lax.all_to_all(send, "tile", 0, 0, tiled=True)
    recv_rows = recv[:, :CAP].reshape(slots, block_width)
    recv_col = recv[:, CAP:CAP + CAP // block_width].reshape(1, slots).astype(jnp.int32)
    jac_ids = lax.broadcasted_iota(jnp.int32, (jac_total, slots), 0)
    binner = (jac_ids == recv_col).astype(jnp.bfloat16)
    summed = jnp.dot(binner, recv_rows, preferred_element_type=jnp.float32)

    merged = summed.astype(jnp.bfloat16)
    group = 16
    groups = jac_total // group
    jac_groups = jacobian[0].reshape(groups, group * block_width, block_width)
    eye = (
        lax.broadcasted_iota(jnp.int32, (group, group), 0)
        == lax.broadcasted_iota(jnp.int32, (group, group), 1)
    ).astype(jnp.bfloat16)
    spread = jnp.einsum("kij,ki->kj", jacobian[0], merged, preferred_element_type=jnp.float32)
    state_ids = lax.broadcasted_iota(jnp.int32, (state_total, jac_total), 0)
    owners = state_ids == jac_state[0][None, :]
    state = jnp.dot(owners.astype(jnp.float32), spread, precision=lax.Precision.HIGHEST).astype(
        jnp.bfloat16
    )
    corr_total = corr_blocks.shape[1]
    read_ids = lax.broadcasted_iota(jnp.int32, (corr_total, state_total), 1)
    reader = (read_ids == corr_col[0][:, None]).astype(jnp.bfloat16)
    source = jnp.dot(reader, state, preferred_element_type=jnp.float32).astype(jnp.bfloat16)
    mixing = jnp.einsum("cij,cj->ci", corr_blocks[0], source, preferred_element_type=jnp.float32)
    write_ids = lax.broadcasted_iota(jnp.int32, (state_total, corr_total), 0)
    writer = (write_ids == corr_row[0][None, :]).astype(jnp.float32)
    spatial = jnp.dot(writer, mixing, precision=lax.Precision.HIGHEST).astype(jnp.bfloat16)
    coupling = time_coupling[0]
    earlier = from_behind(spatial, "tm", 1)
    later_state, later_coupling = from_behind((spatial, coupling), "tm", -1)
    coupled = (
        spatial.astype(jnp.float32)
        + coupling.astype(jnp.float32) * earlier.astype(jnp.float32)
        + later_coupling.astype(jnp.float32) * later_state.astype(jnp.float32)
    ).astype(jnp.bfloat16)
    local_state = jnp.dot(
        owners.T.astype(jnp.bfloat16), coupled, preferred_element_type=jnp.float32
    ).astype(jnp.bfloat16)
    wide = jnp.einsum(
        "gkj,grj->gkr",
        local_state.reshape(groups, group, block_width),
        jac_groups,
        preferred_element_type=jnp.float32,
    ).reshape(groups, group, group, block_width)
    model_obs = (
        jnp.sum(wide * eye.astype(jnp.float32)[None, :, :, None], axis=2)
        .reshape(jac_total, block_width)
        .astype(jnp.bfloat16)
    )

    answer = jnp.dot(binner.T, model_obs, preferred_element_type=jnp.float32).astype(jnp.bfloat16)
    back = lax.all_to_all(answer.reshape(tiles, CAP, block_width), "tile", 0, 0, tiled=True)
    gathered = jnp.take(back.reshape(slots, block_width), slot, axis=0, mode="clip").astype(jnp.float32)
    return (gathered * keeping).astype(jnp.bfloat16)[None]


def solution(mesh):
    in_specs = (
        P("tm", "tile", None),
        P("tm", "tile", None),
        P("tm", "tile"),
        P("tm", "tile", None),
        P("tm", "tile"),
        P("tm", "tile", None, None),
        P("tm", "tile"),
        P("tm", "tile", None, None),
        P("tm", "tile"),
        P("tm", "tile"),
        P("tm", "tile", None),
    )
    out_specs = P("tm", "tile", None)
    return jax.shard_map(shards, mesh=mesh, in_specs=in_specs, out_specs=out_specs, check_vma=False)
```

```python
import jax
import jax.numpy as jnp
from jax import lax
from jax.sharding import PartitionSpec as P

CAP = 256


def from_behind(x, axis, by):
    length = lax.axis_size(axis)
    pairs = [(i, i + by) for i in range(length) if 0 <= i + by < length]
    return lax.ppermute(x, axis, pairs)


def shards(
    obs_values,
    obs_weight,
    obs_count,
    dest_tile,
    jac_index,
    jacobian,
    jac_state,
    corr_blocks,
    corr_row,
    corr_col,
    time_coupling,
):
    obs_total = obs_values.shape[1]
    block_width = obs_values.shape[2]
    jac_total = jacobian.shape[1]
    state_total = time_coupling.shape[1]
    tiles = lax.axis_size("tile")
    slots = tiles * CAP
    lane_index = lax.broadcasted_iota(jnp.int32, (obs_total, block_width), 1)
    keeping = (lane_index < obs_count[0][:, None]).astype(jnp.float32)
    weighted = (
        obs_values[0].astype(jnp.float32) * obs_weight[0].astype(jnp.float32) * keeping
    ).astype(jnp.bfloat16)
    target = dest_tile[0, :, 0]
    column = jac_index[0]

    tile_ids = lax.broadcasted_iota(jnp.int32, (obs_total, tiles), 1)
    names = (tile_ids == target[:, None]).astype(jnp.bfloat16)
    chunk = 128
    pieces = obs_total // chunk
    rows = lax.broadcasted_iota(jnp.int32, (chunk, chunk), 0)
    cols = lax.broadcasted_iota(jnp.int32, (chunk, chunk), 1)
    lower = (cols <= rows).astype(jnp.bfloat16)
    names_c = names.reshape(pieces, chunk, tiles)
    within = jnp.einsum("rc,pct->prt", lower, names_c, preferred_element_type=jnp.float32)
    totals = within[:, chunk - 1, :]
    before = jnp.cumsum(totals, axis=0) - totals
    counts = (within + before[:, None, :]).reshape(obs_total, tiles)
    rank = jnp.sum(counts * names.astype(jnp.float32), axis=1).astype(jnp.int32) - 1
    slot = target * CAP + rank

    rank_ids = lax.broadcasted_iota(jnp.int32, (obs_total, CAP), 1)
    ranked = (rank_ids == rank[:, None]).astype(jnp.bfloat16)
    labels = jnp.concatenate(
        [column.astype(jnp.bfloat16)[:, None], obs_count[0].astype(jnp.bfloat16)[:, None]], axis=1
    )
    packed_meta = jnp.einsum(
        "jd,jr,jm->dmr", names, ranked, labels, preferred_element_type=jnp.float32
    ).astype(jnp.bfloat16)
    masked = jnp.where(
        (tile_ids == target[:, None]).T[:, :, None], weighted[None], jnp.zeros((), jnp.bfloat16)
    )
    packed = jnp.einsum(
        "jr,djc->drc", ranked, masked, preferred_element_type=jnp.float32
    ).astype(jnp.bfloat16)
    send = jnp.concatenate(
        [
            packed.reshape(tiles, CAP, block_width),
            packed_meta.reshape(tiles, 2 * CAP // block_width, block_width),
            jnp.zeros((tiles, 16 - 2 * CAP // block_width, block_width), jnp.bfloat16),
        ],
        axis=1,
    )
    recv = lax.all_to_all(send, "tile", 0, 0, tiled=True)
    recv_rows = recv[:, :CAP].reshape(slots, block_width)
    recv_col = recv[:, CAP:CAP + CAP // block_width].reshape(1, slots).astype(jnp.int32)
    jac_ids = lax.broadcasted_iota(jnp.int32, (jac_total, slots), 0)
    binner = (jac_ids == recv_col).astype(jnp.bfloat16)
    recv_count = recv[:, CAP + CAP // block_width:CAP + 2 * CAP // block_width].reshape(slots, 1).astype(jnp.int32)
    slot_lanes = lax.broadcasted_iota(jnp.int32, (slots, block_width), 1)
    slot_keep = (slot_lanes < recv_count).astype(jnp.float32)
    summed = jnp.dot(binner, recv_rows, preferred_element_type=jnp.float32)

    merged = summed.astype(jnp.bfloat16)
    group = 16
    groups = jac_total // group
    jac_groups = jacobian[0].reshape(groups, group * block_width, block_width)
    eye = (
        lax.broadcasted_iota(jnp.int32, (group, group), 0)
        == lax.broadcasted_iota(jnp.int32, (group, group), 1)
    ).astype(jnp.bfloat16)
    spread = jnp.einsum("kij,ki->kj", jacobian[0], merged, preferred_element_type=jnp.float32)
    state_ids = lax.broadcasted_iota(jnp.int32, (state_total, jac_total), 0)
    owners = state_ids == jac_state[0][None, :]
    state = jnp.dot(owners.astype(jnp.float32), spread, precision=lax.Precision.HIGHEST).astype(
        jnp.bfloat16
    )
    corr_total = corr_blocks.shape[1]
    read_ids = lax.broadcasted_iota(jnp.int32, (corr_total, state_total), 1)
    reader = (read_ids == corr_col[0][:, None]).astype(jnp.bfloat16)
    source = jnp.dot(reader, state, preferred_element_type=jnp.float32).astype(jnp.bfloat16)
    mixing = jnp.einsum("cij,cj->ci", corr_blocks[0], source, preferred_element_type=jnp.float32)
    write_ids = lax.broadcasted_iota(jnp.int32, (state_total, corr_total), 0)
    writer = (write_ids == corr_row[0][None, :]).astype(jnp.float32)
    spatial = jnp.dot(writer, mixing, precision=lax.Precision.HIGHEST).astype(jnp.bfloat16)
    coupling = time_coupling[0]
    earlier = from_behind(spatial, "tm", 1)
    later_state, later_coupling = from_behind((spatial, coupling), "tm", -1)
    coupled = (
        spatial.astype(jnp.float32)
        + coupling.astype(jnp.float32) * earlier.astype(jnp.float32)
        + later_coupling.astype(jnp.float32) * later_state.astype(jnp.float32)
    ).astype(jnp.bfloat16)
    local_state = jnp.dot(
        owners.T.astype(jnp.bfloat16), coupled, preferred_element_type=jnp.float32
    ).astype(jnp.bfloat16)
    wide = jnp.einsum(
        "gkj,grj->gkr",
        local_state.reshape(groups, group, block_width),
        jac_groups,
        preferred_element_type=jnp.float32,
    ).reshape(groups, group, group, block_width)
    model_obs = (
        jnp.sum(wide * eye.astype(jnp.float32)[None, :, :, None], axis=2)
        .reshape(jac_total, block_width)
        .astype(jnp.bfloat16)
    )

    answer = (
        jnp.dot(binner.T, model_obs, preferred_element_type=jnp.float32) * slot_keep
    ).astype(jnp.bfloat16)
    back = lax.all_to_all(answer.reshape(tiles, CAP, block_width), "tile", 0, 0, tiled=True)
    gathered = jnp.take(back.reshape(slots, block_width), slot, axis=0, mode="clip")
    return gathered[None]


def solution(mesh):
    in_specs = (
        P("tm", "tile", None),
        P("tm", "tile", None),
        P("tm", "tile"),
        P("tm", "tile", None),
        P("tm", "tile"),
        P("tm", "tile", None, None),
        P("tm", "tile"),
        P("tm", "tile", None, None),
        P("tm", "tile"),
        P("tm", "tile"),
        P("tm", "tile", None),
    )
    out_specs = P("tm", "tile", None)
    return jax.shard_map(shards, mesh=mesh, in_specs=in_specs, out_specs=out_specs, check_vma=False)
```

```python
import jax
import jax.numpy as jnp
from jax import lax
from jax.sharding import PartitionSpec as P

CAP = 256


def from_behind(x, axis, by):
    length = lax.axis_size(axis)
    pairs = [(i, i + by) for i in range(length) if 0 <= i + by < length]
    return lax.ppermute(x, axis, pairs)


def shards(
    obs_values,
    obs_weight,
    obs_count,
    dest_tile,
    jac_index,
    jacobian,
    jac_state,
    corr_blocks,
    corr_row,
    corr_col,
    time_coupling,
):
    obs_total = obs_values.shape[1]
    block_width = obs_values.shape[2]
    jac_total = jacobian.shape[1]
    state_total = time_coupling.shape[1]
    tiles = lax.axis_size("tile")
    slots = tiles * CAP
    lane_index = lax.broadcasted_iota(jnp.int32, (obs_total, block_width), 1)
    keeping = (lane_index < obs_count[0][:, None]).astype(jnp.float32)
    weighted = (
        obs_values[0].astype(jnp.float32) * obs_weight[0].astype(jnp.float32) * keeping
    ).astype(jnp.bfloat16)
    target = dest_tile[0, :, 0]
    column = jac_index[0]

    tile_ids = lax.broadcasted_iota(jnp.int32, (obs_total, tiles), 1)
    names = (tile_ids == target[:, None]).astype(jnp.bfloat16)
    chunk = 128
    pieces = obs_total // chunk
    rows = lax.broadcasted_iota(jnp.int32, (chunk, chunk), 0)
    cols = lax.broadcasted_iota(jnp.int32, (chunk, chunk), 1)
    lower = (cols <= rows).astype(jnp.bfloat16)
    names_c = names.reshape(pieces, chunk, tiles)
    within = jnp.einsum("rc,pct->prt", lower, names_c, preferred_element_type=jnp.float32)
    totals = within[:, chunk - 1, :]
    earlier_piece = (
        lax.broadcasted_iota(jnp.int32, (pieces, pieces), 1)
        < lax.broadcasted_iota(jnp.int32, (pieces, pieces), 0)
    ).astype(jnp.float32)
    before = jnp.dot(earlier_piece, totals, precision=lax.Precision.HIGHEST)
    counts = (within + before[:, None, :]).reshape(obs_total, tiles)
    rank = jnp.sum(counts * names.astype(jnp.float32), axis=1).astype(jnp.int32) - 1
    slot = target * CAP + rank

    rank_ids = lax.broadcasted_iota(jnp.int32, (obs_total, CAP), 1)
    ranked = (rank_ids == rank[:, None]).astype(jnp.bfloat16)
    packed_col = jnp.dot(
        (names * column.astype(jnp.bfloat16)[:, None]).T, ranked, preferred_element_type=jnp.float32
    ).astype(jnp.bfloat16)
    masked = jnp.where(
        (tile_ids == target[:, None]).T[:, :, None], weighted[None], jnp.zeros((), jnp.bfloat16)
    )
    packed = jnp.einsum(
        "jr,djc->drc", ranked, masked, preferred_element_type=jnp.float32
    ).astype(jnp.bfloat16)
    send = jnp.concatenate(
        [
            packed.reshape(tiles, CAP, block_width),
            packed_col.reshape(tiles, CAP // block_width, block_width),
            jnp.zeros((tiles, 16 - CAP // block_width, block_width), jnp.bfloat16),
        ],
        axis=1,
    )
    recv = lax.all_to_all(send, "tile", 0, 0, tiled=True)
    recv_rows = recv[:, :CAP].reshape(slots, block_width)
    recv_col = recv[:, CAP:CAP + CAP // block_width].reshape(1, slots).astype(jnp.int32)
    jac_ids = lax.broadcasted_iota(jnp.int32, (jac_total, slots), 0)
    binner = (jac_ids == recv_col).astype(jnp.bfloat16)
    summed = jnp.dot(binner, recv_rows, preferred_element_type=jnp.float32)

    merged = summed.astype(jnp.bfloat16)
    group = 16
    groups = jac_total // group
    jac_groups = jacobian[0].reshape(groups, group * block_width, block_width)
    eye = (
        lax.broadcasted_iota(jnp.int32, (group, group), 0)
        == lax.broadcasted_iota(jnp.int32, (group, group), 1)
    ).astype(jnp.bfloat16)
    spread = jnp.einsum("kij,ki->kj", jacobian[0], merged, preferred_element_type=jnp.float32)
    state_ids = lax.broadcasted_iota(jnp.int32, (state_total, jac_total), 0)
    owners = state_ids == jac_state[0][None, :]
    state = jnp.dot(owners.astype(jnp.float32), spread, precision=lax.Precision.HIGHEST).astype(
        jnp.bfloat16
    )
    corr_total = corr_blocks.shape[1]
    read_ids = lax.broadcasted_iota(jnp.int32, (corr_total, state_total), 1)
    reader = (read_ids == corr_col[0][:, None]).astype(jnp.bfloat16)
    source = jnp.dot(reader, state, preferred_element_type=jnp.float32).astype(jnp.bfloat16)
    mixing = jnp.einsum("cij,cj->ci", corr_blocks[0], source, preferred_element_type=jnp.float32)
    write_ids = lax.broadcasted_iota(jnp.int32, (state_total, corr_total), 0)
    writer = (write_ids == corr_row[0][None, :]).astype(jnp.float32)
    spatial = jnp.dot(writer, mixing, precision=lax.Precision.HIGHEST).astype(jnp.bfloat16)
    coupling = time_coupling[0]
    earlier = from_behind(spatial, "tm", 1)
    later_state, later_coupling = from_behind((spatial, coupling), "tm", -1)
    coupled = (
        spatial.astype(jnp.float32)
        + coupling.astype(jnp.float32) * earlier.astype(jnp.float32)
        + later_coupling.astype(jnp.float32) * later_state.astype(jnp.float32)
    ).astype(jnp.bfloat16)
    local_state = jnp.dot(
        owners.T.astype(jnp.bfloat16), coupled, preferred_element_type=jnp.float32
    ).astype(jnp.bfloat16)
    wide = jnp.einsum(
        "gkj,grj->gkr",
        local_state.reshape(groups, group, block_width),
        jac_groups,
        preferred_element_type=jnp.float32,
    ).reshape(groups, group, group, block_width)
    model_obs = (
        jnp.sum(wide * eye.astype(jnp.float32)[None, :, :, None], axis=2)
        .reshape(jac_total, block_width)
        .astype(jnp.bfloat16)
    )

    answer = jnp.dot(binner.T, model_obs, preferred_element_type=jnp.float32).astype(jnp.bfloat16)
    back = lax.all_to_all(answer.reshape(tiles, CAP, block_width), "tile", 0, 0, tiled=True)
    gathered = jnp.take(back.reshape(slots, block_width), slot, axis=0, mode="clip").astype(jnp.float32)
    return (gathered * keeping).astype(jnp.bfloat16)[None]


def solution(mesh):
    in_specs = (
        P("tm", "tile", None),
        P("tm", "tile", None),
        P("tm", "tile"),
        P("tm", "tile", None),
        P("tm", "tile"),
        P("tm", "tile", None, None),
        P("tm", "tile"),
        P("tm", "tile", None, None),
        P("tm", "tile"),
        P("tm", "tile"),
        P("tm", "tile", None),
    )
    out_specs = P("tm", "tile", None)
    return jax.shard_map(shards, mesh=mesh, in_specs=in_specs, out_specs=out_specs, check_vma=False)
```

```python
import jax
import jax.numpy as jnp
from jax import lax
from jax.sharding import PartitionSpec as P

CAP = 256


def from_behind(x, axis, by):
    length = lax.axis_size(axis)
    pairs = [(i, i + by) for i in range(length) if 0 <= i + by < length]
    return lax.ppermute(x, axis, pairs)


def shards(
    obs_values,
    obs_weight,
    obs_count,
    dest_tile,
    jac_index,
    jacobian,
    jac_state,
    corr_blocks,
    corr_row,
    corr_col,
    time_coupling,
):
    obs_total = obs_values.shape[1]
    block_width = obs_values.shape[2]
    jac_total = jacobian.shape[1]
    state_total = time_coupling.shape[1]
    tiles = lax.axis_size("tile")
    slots = tiles * CAP
    lane_index = lax.broadcasted_iota(jnp.int32, (obs_total, block_width), 1)
    keeping = (lane_index < obs_count[0][:, None]).astype(jnp.float32)
    weighted = (
        obs_values[0].astype(jnp.float32) * obs_weight[0].astype(jnp.float32) * keeping
    ).astype(jnp.bfloat16)
    target = dest_tile[0, :, 0]
    column = jac_index[0]

    tile_ids = lax.broadcasted_iota(jnp.int32, (obs_total, tiles), 1)
    names = (tile_ids == target[:, None]).astype(jnp.bfloat16)
    chunk = 128
    pieces = obs_total // chunk
    rows = lax.broadcasted_iota(jnp.int32, (chunk, chunk), 0)
    cols = lax.broadcasted_iota(jnp.int32, (chunk, chunk), 1)
    lower = (cols <= rows).astype(jnp.bfloat16)
    names_c = names.reshape(pieces, chunk, tiles)
    within = jnp.einsum("rc,pct->prt", lower, names_c, preferred_element_type=jnp.float32)
    totals = within[:, chunk - 1, :]
    earlier_piece = (
        lax.broadcasted_iota(jnp.int32, (pieces, pieces), 1)
        < lax.broadcasted_iota(jnp.int32, (pieces, pieces), 0)
    ).astype(jnp.float32)
    before = jnp.dot(earlier_piece, totals, precision=lax.Precision.HIGHEST)
    counts = (within + before[:, None, :]).reshape(obs_total, tiles)
    rank = jnp.sum(counts * names.astype(jnp.float32), axis=1).astype(jnp.int32) - 1
    slot = target * CAP + rank

    rank_ids = lax.broadcasted_iota(jnp.int32, (obs_total, CAP), 1)
    ranked = (rank_ids == rank[:, None]).astype(jnp.bfloat16)
    packed_col = jnp.dot(
        (names * column.astype(jnp.bfloat16)[:, None]).T, ranked, preferred_element_type=jnp.float32
    ).astype(jnp.bfloat16)
    masked = jnp.where(
        (tile_ids == target[:, None]).T[:, :, None], weighted[None], jnp.zeros((), jnp.bfloat16)
    )
    packed = jnp.einsum(
        "jr,djc->drc", ranked, masked, preferred_element_type=jnp.float32
    ).astype(jnp.bfloat16)
    send = jnp.concatenate(
        [
            packed.reshape(tiles, CAP, block_width),
            packed_col.reshape(tiles, CAP // block_width, block_width),
            jnp.zeros((tiles, 16 - CAP // block_width, block_width), jnp.bfloat16),
        ],
        axis=1,
    )
    recv = lax.all_to_all(send, "tile", 0, 0, tiled=True)
    recv_rows = recv[:, :CAP].reshape(slots, block_width)
    recv_col = recv[:, CAP:CAP + CAP // block_width].reshape(1, slots).astype(jnp.int32)
    jac_ids = lax.broadcasted_iota(jnp.int32, (jac_total, slots), 0)
    binner = (jac_ids == recv_col).astype(jnp.bfloat16)
    summed = jnp.dot(binner, recv_rows, preferred_element_type=jnp.float32)

    merged = summed.astype(jnp.bfloat16)
    group = 16
    groups = jac_total // group
    jac_groups = jacobian[0].reshape(groups, group * block_width, block_width)
    eye = (
        lax.broadcasted_iota(jnp.int32, (group, group), 0)
        == lax.broadcasted_iota(jnp.int32, (group, group), 1)
    ).astype(jnp.bfloat16)
    spread = jnp.einsum("kij,ki->kj", jacobian[0], merged, preferred_element_type=jnp.float32)
    state_ids = lax.broadcasted_iota(jnp.int32, (state_total, jac_total), 0)
    owners = state_ids == jac_state[0][None, :]
    state = jnp.dot(owners.astype(jnp.float32), spread, precision=lax.Precision.HIGHEST).astype(
        jnp.bfloat16
    )
    corr_total = corr_blocks.shape[1]
    read_ids = lax.broadcasted_iota(jnp.int32, (corr_total, state_total), 1)
    reader = (read_ids == corr_col[0][:, None]).astype(jnp.bfloat16)
    source = jnp.dot(reader, state, preferred_element_type=jnp.float32).astype(jnp.bfloat16)
    mixing = jnp.einsum("cij,cj->ci", corr_blocks[0], source, preferred_element_type=jnp.float32)
    write_ids = lax.broadcasted_iota(jnp.int32, (state_total, corr_total), 0)
    writer = (write_ids == corr_row[0][None, :]).astype(jnp.float32)
    spatial = jnp.dot(writer, mixing, precision=lax.Precision.HIGHEST).astype(jnp.bfloat16)
    coupling = time_coupling[0]
    earlier = from_behind(spatial, "tm", 1)
    later_state, later_coupling = from_behind((spatial, coupling), "tm", -1)
    coupled = (
        spatial.astype(jnp.float32)
        + coupling.astype(jnp.float32) * earlier.astype(jnp.float32)
        + later_coupling.astype(jnp.float32) * later_state.astype(jnp.float32)
    ).astype(jnp.bfloat16)
    local_state = jnp.dot(
        owners.T.astype(jnp.bfloat16), coupled, preferred_element_type=jnp.float32
    ).astype(jnp.bfloat16)
    wide = jnp.einsum(
        "gkj,grj->gkr",
        local_state.reshape(groups, group, block_width),
        jac_groups,
        preferred_element_type=jnp.float32,
    ).astype(jnp.bfloat16).reshape(groups, group, group, block_width)
    model_obs = (
        jnp.sum(
            jnp.where(eye[None, :, :, None] > 0, wide, jnp.zeros((), jnp.bfloat16)).astype(jnp.float32),
            axis=2,
        )
        .reshape(jac_total, block_width)
        .astype(jnp.bfloat16)
    )

    answer = jnp.dot(binner.T, model_obs, preferred_element_type=jnp.float32).astype(jnp.bfloat16)
    back = lax.all_to_all(answer.reshape(tiles, CAP, block_width), "tile", 0, 0, tiled=True)
    gathered = jnp.take(back.reshape(slots, block_width), slot, axis=0, mode="clip").astype(jnp.float32)
    return (gathered * keeping).astype(jnp.bfloat16)[None]


def solution(mesh):
    in_specs = (
        P("tm", "tile", None),
        P("tm", "tile", None),
        P("tm", "tile"),
        P("tm", "tile", None),
        P("tm", "tile"),
        P("tm", "tile", None, None),
        P("tm", "tile"),
        P("tm", "tile", None, None),
        P("tm", "tile"),
        P("tm", "tile"),
        P("tm", "tile", None),
    )
    out_specs = P("tm", "tile", None)
    return jax.shard_map(shards, mesh=mesh, in_specs=in_specs, out_specs=out_specs, check_vma=False)
```

```python
import jax
import jax.numpy as jnp
from jax import lax
from jax.sharding import PartitionSpec as P

CAP = 256


def from_behind(x, axis, by):
    length = lax.axis_size(axis)
    pairs = [(i, i + by) for i in range(length) if 0 <= i + by < length]
    return lax.ppermute(x, axis, pairs)


def shards(
    obs_values,
    obs_weight,
    obs_count,
    dest_tile,
    jac_index,
    jacobian,
    jac_state,
    corr_blocks,
    corr_row,
    corr_col,
    time_coupling,
):
    obs_total = obs_values.shape[1]
    block_width = obs_values.shape[2]
    jac_total = jacobian.shape[1]
    state_total = time_coupling.shape[1]
    tiles = lax.axis_size("tile")
    slots = tiles * CAP
    lane_index = lax.broadcasted_iota(jnp.int32, (obs_total, block_width), 1)
    keeping = (lane_index < obs_count[0][:, None]).astype(jnp.float32)
    weighted = (
        obs_values[0].astype(jnp.float32) * obs_weight[0].astype(jnp.float32) * keeping
    ).astype(jnp.bfloat16)
    target = dest_tile[0, :, 0]
    column = jac_index[0]

    tile_ids = lax.broadcasted_iota(jnp.int32, (obs_total, tiles), 1)
    names = (tile_ids == target[:, None]).astype(jnp.bfloat16)
    chunk = 128
    pieces = obs_total // chunk
    rows = lax.broadcasted_iota(jnp.int32, (chunk, chunk), 0)
    cols = lax.broadcasted_iota(jnp.int32, (chunk, chunk), 1)
    lower = (cols <= rows).astype(jnp.bfloat16)
    names_c = names.reshape(pieces, chunk, tiles)
    within = jnp.einsum("rc,pct->prt", lower, names_c, preferred_element_type=jnp.float32)
    totals = within[:, chunk - 1, :]
    earlier_piece = (
        lax.broadcasted_iota(jnp.int32, (pieces, pieces), 1)
        < lax.broadcasted_iota(jnp.int32, (pieces, pieces), 0)
    ).astype(jnp.float32)
    before = jnp.dot(earlier_piece, totals, precision=lax.Precision.HIGHEST)
    counts = (within + before[:, None, :]).reshape(obs_total, tiles)
    rank = jnp.sum(counts * names.astype(jnp.float32), axis=1).astype(jnp.int32) - 1
    slot = target * CAP + rank

    rank_ids = lax.broadcasted_iota(jnp.int32, (obs_total, CAP), 1)
    ranked = (rank_ids == rank[:, None]).astype(jnp.bfloat16)
    packed_col = jnp.dot(
        (names * column.astype(jnp.bfloat16)[:, None]).T, ranked, preferred_element_type=jnp.float32
    ).astype(jnp.bfloat16)
    masked = jnp.where(
        (tile_ids == target[:, None]).T[:, :, None], weighted[None], jnp.zeros((), jnp.bfloat16)
    )
    packed = jnp.einsum(
        "jr,djc->drc", ranked, masked, preferred_element_type=jnp.float32
    ).astype(jnp.bfloat16)
    send = jnp.concatenate(
        [
            packed.reshape(tiles, CAP, block_width),
            packed_col.reshape(tiles, CAP // block_width, block_width),
            jnp.zeros((tiles, 16 - CAP // block_width, block_width), jnp.bfloat16),
        ],
        axis=1,
    )
    recv = lax.all_to_all(send, "tile", 0, 0, tiled=True)
    recv_rows = recv[:, :CAP].reshape(slots, block_width)
    recv_col = recv[:, CAP:CAP + CAP // block_width].reshape(1, slots).astype(jnp.int32)
    jac_ids = lax.broadcasted_iota(jnp.int32, (jac_total, slots), 0)
    binner = (jac_ids == recv_col).astype(jnp.bfloat16)
    summed = jnp.dot(binner, recv_rows, preferred_element_type=jnp.float32)

    merged = summed.astype(jnp.bfloat16)
    group = 16
    groups = jac_total // group
    jac_groups = jacobian[0].reshape(groups, group * block_width, block_width)
    eye = (
        lax.broadcasted_iota(jnp.int32, (group, group), 0)
        == lax.broadcasted_iota(jnp.int32, (group, group), 1)
    ).astype(jnp.bfloat16)
    replicate = (
        lax.broadcasted_iota(jnp.int32, (block_width, group * block_width), 0)
        == lax.broadcasted_iota(jnp.int32, (block_width, group * block_width), 1) % block_width
    ).astype(jnp.bfloat16)
    tiled = jnp.dot(merged, replicate, preferred_element_type=jnp.float32).astype(jnp.bfloat16)
    block_of = lax.broadcasted_iota(jnp.int32, (groups, group, group * block_width), 2) // block_width
    own_block = lax.broadcasted_iota(jnp.int32, (groups, group, group * block_width), 1)
    spread_left = jnp.where(
        block_of == own_block, tiled.reshape(groups, group, group * block_width), jnp.zeros((), jnp.bfloat16)
    )
    spread = jnp.einsum(
        "gkr,grj->gkj", spread_left, jac_groups, preferred_element_type=jnp.float32
    ).reshape(jac_total, block_width)
    state_ids = lax.broadcasted_iota(jnp.int32, (state_total, jac_total), 0)
    owners = state_ids == jac_state[0][None, :]
    state = jnp.dot(owners.astype(jnp.float32), spread, precision=lax.Precision.HIGHEST).astype(
        jnp.bfloat16
    )
    corr_total = corr_blocks.shape[1]
    read_ids = lax.broadcasted_iota(jnp.int32, (corr_total, state_total), 1)
    reader = (read_ids == corr_col[0][:, None]).astype(jnp.bfloat16)
    source = jnp.dot(reader, state, preferred_element_type=jnp.float32).astype(jnp.bfloat16)
    mixing = jnp.einsum("cij,cj->ci", corr_blocks[0], source, preferred_element_type=jnp.float32)
    write_ids = lax.broadcasted_iota(jnp.int32, (state_total, corr_total), 0)
    writer = (write_ids == corr_row[0][None, :]).astype(jnp.float32)
    spatial = jnp.dot(writer, mixing, precision=lax.Precision.HIGHEST).astype(jnp.bfloat16)
    coupling = time_coupling[0]
    earlier = from_behind(spatial, "tm", 1)
    later_state, later_coupling = from_behind((spatial, coupling), "tm", -1)
    coupled = (
        spatial.astype(jnp.float32)
        + coupling.astype(jnp.float32) * earlier.astype(jnp.float32)
        + later_coupling.astype(jnp.float32) * later_state.astype(jnp.float32)
    ).astype(jnp.bfloat16)
    local_state = jnp.dot(
        owners.T.astype(jnp.bfloat16), coupled, preferred_element_type=jnp.float32
    ).astype(jnp.bfloat16)
    wide = jnp.einsum(
        "gkj,grj->gkr",
        local_state.reshape(groups, group, block_width),
        jac_groups,
        preferred_element_type=jnp.float32,
    ).reshape(groups, group, group, block_width)
    model_obs = (
        jnp.sum(wide * eye.astype(jnp.float32)[None, :, :, None], axis=2)
        .reshape(jac_total, block_width)
        .astype(jnp.bfloat16)
    )

    answer = jnp.dot(binner.T, model_obs, preferred_element_type=jnp.float32).astype(jnp.bfloat16)
    back = lax.all_to_all(answer.reshape(tiles, CAP, block_width), "tile", 0, 0, tiled=True)
    gathered = jnp.take(back.reshape(slots, block_width), slot, axis=0, mode="clip").astype(jnp.float32)
    return (gathered * keeping).astype(jnp.bfloat16)[None]


def solution(mesh):
    in_specs = (
        P("tm", "tile", None),
        P("tm", "tile", None),
        P("tm", "tile"),
        P("tm", "tile", None),
        P("tm", "tile"),
        P("tm", "tile", None, None),
        P("tm", "tile"),
        P("tm", "tile", None, None),
        P("tm", "tile"),
        P("tm", "tile"),
        P("tm", "tile", None),
    )
    out_specs = P("tm", "tile", None)
    return jax.shard_map(shards, mesh=mesh, in_specs=in_specs, out_specs=out_specs, check_vma=False)
```
